32 devices in a mesh: clips: 2 (over y), tm: 4 (over z), height: 4 (over x, core).
Axes of the slice: x: 2, y: 2, z: 4, core: 2. Of those that a mesh axis runs over, the one named last changes fastest.
Arguments:
- clip_frames: bfloat16 [32, 32, 16, 192], P(('clips', 'tm'), 'height'), parts along dimension 0, may hold values from -6 to 6
- w_first: bfloat16 [3, 3, 3, 192, 192], replicated, may hold values from -0.078125 to 0.078125
- b_first: float32 [192], replicated, may hold values from -3 to 3
- w_second: bfloat16 [3, 3, 3, 192, 192], replicated, may hold values from -0.078125 to 0.078125
- b_second: float32 [192], replicated, may hold values from -3 to 3
Outputs:
- block_out: bfloat16 [32, 32, 16, 192], P(('clips', 'tm'), 'height'), parts along dimension 0
The draws below stay inside these ranges and needn't reach their ends.
There are 2 independent parts, one for each index of `clips`. The reference program is written for one: setup_inputs(seed, part) draws one part's arguments, and reference() takes and returns one part's arrays. A program takes and returns all parts, laid end to end along the dimension named above; an argument that names none is the same for every part. Nothing has to cross between parts.
All inputs are finite; a program needn't handle non-finite values.
Results may differ from the reference program's by a relative error of at most 0.003.
Values may be sent and summed in bfloat16 or wider, within the bound.
No kernel may reach another device: no remote copies, remote signals or barrier semaphores. Data moves between devices by JAX's collectives and lax.ppermute only.
A program may use at most 64 MiB of HBM per device.

```python
import jax
import jax.numpy as jnp
from jax import lax

C = 192
COLS = 16
FRAMES = 16
ROWS = 32


def shard_levels(key, dims, cuts, low, high):
    level = 1.0
    for position, parts in cuts:
        heights = jax.random.uniform(jax.random.fold_in(jax.random.fold_in(key, 6), position), (parts,), jnp.float32, low / len(cuts), high / len(cuts))
        level = level * jnp.repeat(jnp.exp(heights), dims[position] // parts).reshape((-1,) + (1,) * (len(dims) - 1 - position))
    return level


def bell_draw(rng, shape, width, bound, shards=(), kind=jnp.bfloat16):
    drawn = jax.random.normal(rng, shape, jnp.float32) * width
    if len(shards) > 0:
        drawn = shard_levels(rng, shape, shards, -0.22, 0.18) * drawn
    return jnp.clip(drawn, min=-bound, max=bound).astype(kind)


def setup_inputs(seed: int = 0, part: int = 0) -> dict:
    key_list = jax.random.split(jax.random.key(seed), 6)
    own_keys = jax.random.split(jax.random.fold_in(key_list[5], part), 6)
    return {
        "clip_frames": bell_draw(own_keys[0], (FRAMES, ROWS, COLS, C), 1.0, 6.0, ((0, 4), (1, 4))),
        "w_first": bell_draw(key_list[1], (3, 3, 3, C, C), (27 * C) ** -0.5, 0.078125),
        "b_first": bell_draw(key_list[2], (C,), 0.5, 3.0, (), jnp.float32),
        "w_second": bell_draw(key_list[3], (3, 3, 3, C, C), (27 * C) ** -0.5, 0.078125),
        "b_second": bell_draw(key_list[4], (C,), 0.5, 3.0, (), jnp.float32),
    }


def conv_valid(padded, weight):
    frame_count = padded.shape[0] - 2
    row_count = padded.shape[1] - 2
    col_count = padded.shape[2] - 2
    chans = weight.shape[3]
    summed = jnp.zeros((frame_count * row_count * col_count, weight.shape[4]), jnp.float32)
    for tap_time in range(3):
        stacked = jnp.concatenate([padded[tap_time:tap_time + frame_count, tap_row:tap_row + row_count, tap_col:tap_col + col_count] for tap_row in range(3) for tap_col in range(3)], -1)
        stacked = stacked.reshape(-1, 9 * chans)
        kernel = weight[tap_time].reshape(9 * chans, weight.shape[4])
        summed = summed + jnp.dot(stacked, kernel, preferred_element_type=jnp.float32)
    return summed.reshape(frame_count, row_count, col_count, weight.shape[4])


def blocked_conv(field, weight):
    frames = field.shape[0]
    padded = jnp.pad(field, ((2, 0), (1, 1), (1, 1), (0, 0)))
    block_len = 4
    block_count = frames // block_len

    def block_conv(block_index):
        window = lax.dynamic_slice_in_dim(padded, (block_index * block_len).astype(jnp.int32), block_len + 2, 0)
        return conv_valid(window, weight)

    outputs = lax.map(block_conv, jnp.arange(block_count, dtype=jnp.int32))
    return outputs.reshape(frames, field.shape[1], field.shape[2], weight.shape[4])


def reference(clip_frames, w_first, b_first, w_second, b_second):
    activated = jax.nn.silu(clip_frames.astype(jnp.float32)).astype(jnp.bfloat16)
    hidden = blocked_conv(activated, w_first) + b_first
    gated = jax.nn.silu(hidden).astype(jnp.bfloat16)
    second = blocked_conv(gated, w_second) + b_second
    return (clip_frames.astype(jnp.float32) + second).astype(jnp.bfloat16)
```

```python
import jax
import jax.numpy as jnp
from jax import lax
from jax.sharding import PartitionSpec as P


def silu(value):
    value = value.astype(jnp.float32)
    return value / (1 + jnp.exp(-value))


def neighbour(value, shifts):
    axes = tuple(axis for axis, _ in shifts)
    sizes = [lax.axis_size(axis) for axis in axes]
    pairs = []
    total = 1
    for size in sizes:
        total *= size
    for source in range(total):
        coords, rest = [], source
        for size in reversed(sizes):
            coords.append(rest % size)
            rest //= size
        coords = coords[::-1]
        target = [c + step for c, (_, step) in zip(coords, shifts)]
        if all(0 <= t < s for t, s in zip(target, sizes)):
            linear = 0
            for t, s in zip(target, sizes):
                linear = linear * s + t
            pairs.append((source, linear))
    return lax.ppermute(value, axes, pairs)


def conv(field, weight):
    return lax.conv_general_dilated(
        field[None],
        weight,
        window_strides=(1, 1, 1),
        padding=((0, 0), (0, 0), (1, 1)),
        dimension_numbers=("NDHWC", "DHWIO", "NDHWC"),
        preferred_element_type=jnp.float32,
    )[0]


def local(clip_frames, w_first, b_first, w_second, b_second):
    frames, rows = clip_frames.shape[0], clip_frames.shape[1]
    x = clip_frames
    top, bottom = x[:, rows - 2 :], x[:, :2]
    earlier = neighbour(x, (("tm", 1),))
    earlier_top = neighbour(top, (("tm", 1), ("height", 1)))
    earlier_bottom = neighbour(bottom, (("tm", 1), ("height", -1)))
    own_top = neighbour(top, (("height", 1),))
    own_bottom = neighbour(bottom, (("height", -1),))
    extended = jnp.concatenate(
        [
            jnp.concatenate([earlier_top, earlier, earlier_bottom], 1),
            jnp.concatenate([own_top, x, own_bottom], 1),
        ],
        0,
    )
    activated = silu(extended).astype(jnp.bfloat16)
    hidden = conv(activated, w_first) + b_first
    frame = lax.axis_index("tm") * frames - 2 + lax.broadcasted_iota(jnp.int32, (frames + 2, 1, 1, 1), 0)
    row = lax.axis_index("height") * rows - 1 + lax.broadcasted_iota(jnp.int32, (1, rows + 2, 1, 1), 1)
    inside = (frame >= 0) & (row >= 0) & (row < rows * lax.axis_size("height"))
    gated = jnp.where(inside, silu(hidden), 0.0).astype(jnp.bfloat16)
    second = conv(gated, w_second)
    return (x.astype(jnp.float32) + second + b_second).astype(jnp.bfloat16)


def solution(mesh):
    return jax.shard_map(
        local,
        mesh=mesh,
        in_specs=(P(("clips", "tm"), "height", None, None), P(), P(), P(), P()),
        out_specs=P(("clips", "tm"), "height", None, None),
        check_vma=False,
    )
```

```python
import jax
import jax.numpy as jnp
from jax import lax
from jax.sharding import PartitionSpec as P


def silu(value):
    value = value.astype(jnp.float32)
    return value / (1 + jnp.exp(-value))


def neighbour(value, shifts):
    axes = tuple(axis for axis, _ in shifts)
    sizes = [lax.axis_size(axis) for axis in axes]
    pairs = []
    total = 1
    for size in sizes:
        total *= size
    for source in range(total):
        coords, rest = [], source
        for size in reversed(sizes):
            coords.append(rest % size)
            rest //= size
        coords = coords[::-1]
        target = [c + step for c, (_, step) in zip(coords, shifts)]
        if all(0 <= t < s for t, s in zip(target, sizes)):
            linear = 0
            for t, s in zip(target, sizes):
                linear = linear * s + t
            pairs.append((source, linear))
    return lax.ppermute(value, axes, pairs)


def conv(field, weight, frames_before, frames_after):
    return lax.conv_general_dilated(
        field[None],
        weight,
        window_strides=(1, 1, 1),
        padding=((frames_before, frames_after), (0, 0), (1, 1)),
        dimension_numbers=("NDHWC", "DHWIO", "NDHWC"),
        preferred_element_type=jnp.float32,
    )[0]


def local(clip_frames, w_first, b_first, w_second, b_second):
    frames, rows = clip_frames.shape[0], clip_frames.shape[1]
    x = clip_frames
    earlier = neighbour(x, (("tm", 1),))
    own = jnp.concatenate(
        [neighbour(x[:, rows - 2 :], (("height", 1),)), x, neighbour(x[:, :2], (("height", -1),))], 1
    )
    own_part = conv(silu(own).astype(jnp.bfloat16), w_first, 2, 0)
    earlier = jnp.concatenate(
        [
            neighbour(earlier[:, rows - 2 :], (("height", 1),)),
            earlier,
            neighbour(earlier[:, :2], (("height", -1),)),
        ],
        1,
    )
    earlier_part = conv(silu(earlier).astype(jnp.bfloat16), w_first, 0, 2)
    hidden = jnp.concatenate(
        [earlier_part[:2], earlier_part[2:] + own_part[:2], own_part[2:]], 0
    ) + b_first
    frame = lax.axis_index("tm") * frames - 2 + lax.broadcasted_iota(jnp.int32, (frames + 2, 1, 1, 1), 0)
    row = lax.axis_index("height") * rows - 1 + lax.broadcasted_iota(jnp.int32, (1, rows + 2, 1, 1), 1)
    inside = (frame >= 0) & (row >= 0) & (row < rows * lax.axis_size("height"))
    gated = jnp.where(inside, silu(hidden), 0.0).astype(jnp.bfloat16)
    second = conv(gated, w_second, 0, 0)
    return (x.astype(jnp.float32) + second + b_second).astype(jnp.bfloat16)


def solution(mesh):
    return jax.shard_map(
        local,
        mesh=mesh,
        in_specs=(P(("clips", "tm"), "height", None, None), P(), P(), P(), P()),
        out_specs=P(("clips", "tm"), "height", None, None),
        check_vma=False,
    )
```

```python
import jax
import jax.numpy as jnp
from jax import lax
from jax.sharding import PartitionSpec as P


def silu(value):
    value = value.astype(jnp.float32)
    return value / (1 + jnp.exp(-value))


def neighbour(value, shifts):
    axes = tuple(axis for axis, _ in shifts)
    sizes = [lax.axis_size(axis) for axis in axes]
    pairs = []
    total = 1
    for size in sizes:
        total *= size
    for source in range(total):
        coords, rest = [], source
        for size in reversed(sizes):
            coords.append(rest % size)
            rest //= size
        coords = coords[::-1]
        target = [c + step for c, (_, step) in zip(coords, shifts)]
        if all(0 <= t < s for t, s in zip(target, sizes)):
            linear = 0
            for t, s in zip(target, sizes):
                linear = linear * s + t
            pairs.append((source, linear))
    return lax.ppermute(value, axes, pairs)


def conv(field, weight, frames_before, frames_after):
    return lax.conv_general_dilated(
        field[None],
        weight,
        window_strides=(1, 1, 1),
        padding=((frames_before, frames_after), (0, 0), (1, 1)),
        dimension_numbers=("NDHWC", "DHWIO", "NDHWC"),
        preferred_element_type=jnp.float32,
    )[0]


def local(clip_frames, w_first, b_first, w_second, b_second):
    frames, rows = clip_frames.shape[0], clip_frames.shape[1]
    x = clip_frames
    extended = jnp.concatenate([neighbour(x, (("tm", 1),)), x], 0)
    extended = jnp.concatenate(
        [
            neighbour(extended[:, rows - 2 :], (("height", 1),)),
            extended,
            neighbour(extended[:, :2], (("height", -1),)),
        ],
        1,
    )
    hidden = conv(silu(extended).astype(jnp.bfloat16), w_first, 0, 0) + b_first
    frame = lax.axis_index("tm") * frames - 2 + lax.broadcasted_iota(jnp.int32, (frames + 2, 1, 1, 1), 0)
    row = lax.axis_index("height") * rows - 1 + lax.broadcasted_iota(jnp.int32, (1, rows + 2, 1, 1), 1)
    inside = (frame >= 0) & (row >= 0) & (row < rows * lax.axis_size("height"))
    gated = jnp.where(inside, silu(hidden), 0.0).astype(jnp.bfloat16)
    second = conv(gated, w_second, 0, 0)
    return (x.astype(jnp.float32) + second + b_second).astype(jnp.bfloat16)


def solution(mesh):
    return jax.shard_map(
        local,
        mesh=mesh,
        in_specs=(P(("clips", "tm"), "height", None, None), P(), P(), P(), P()),
        out_specs=P(("clips", "tm"), "height", None, None),
        check_vma=False,
    )
```

```python
import functools

import jax
import jax.numpy as jnp
from jax import lax
from jax.experimental import pallas as pl
from jax.experimental.pallas import tpu as pltpu
from jax.sharding import PartitionSpec as P


def silu(value):
    value = value.astype(jnp.float32)
    return value / (1 + jnp.exp(-value))


def neighbour(value, axis, step):
    size = lax.axis_size(axis)
    pairs = [(i, i + step) for i in range(size) if 0 <= i + step < size]
    return lax.ppermute(value, axis, pairs)


def column_taps(flat, cols, store):
    count = flat.shape[0]
    col = lax.broadcasted_iota(jnp.int32, flat.shape, 0) % cols
    store(0, jnp.where(col == 0, 0.0, pltpu.roll(flat, 1, 0)).astype(jnp.bfloat16))
    store(1, flat.astype(jnp.bfloat16))
    store(2, jnp.where(col == cols - 1, 0.0, pltpu.roll(flat, count - 1, 0)).astype(jnp.bfloat16))


def conv_taps(taps, weight, frames, rows):
    cols, chans = taps.shape[3], taps.shape[4]
    total = None
    for a in range(3):
        for b in range(3):
            for e in range(3):
                lhs = taps[e, a : a + frames, b : b + rows].reshape(frames * rows * cols, chans)
                term = jnp.dot(lhs, weight[(a * 3 + b) * 3 + e], preferred_element_type=jnp.float32)
                total = term if total is None else total + term
    return total


def block_kernel(flags, earlier, own, top, bottom, w_first, b_first, w_second, b_second, out, field, taps1, taps2):
    frames, rows, cols, chans = own.shape
    field[0:frames, 2 : rows + 2] = silu(earlier[...])
    field[frames:, 2 : rows + 2] = silu(own[...])
    field[:, 0:2] = silu(top[...])
    field[:, rows + 2 :] = silu(bottom[...])
    flat = field[...].reshape(2 * frames * (rows + 4) * cols, chans)

    def store1(e, value):
        taps1[e] = value.reshape(2 * frames, rows + 4, cols, chans)

    column_taps(flat, cols, store1)
    hidden = conv_taps(taps1, w_first, frames + 2, rows + 2) + b_first[...]

    def store2(e, value):
        taps2[e] = value.reshape(frames + 2, rows + 2, cols, chans)

    column_taps(silu(hidden), cols, store2)

    @pl.when(flags[0] != 0)
    def _():
        taps2[:, 0:2] = jnp.zeros((3, 2, rows + 2, cols, chans), jnp.bfloat16)

    @pl.when(flags[1] != 0)
    def _():
        taps2[:, :, 0:1] = jnp.zeros((3, frames + 2, 1, cols, chans), jnp.bfloat16)

    @pl.when(flags[2] != 0)
    def _():
        taps2[:, :, rows + 1 :] = jnp.zeros((3, frames + 2, 1, cols, chans), jnp.bfloat16)

    second = conv_taps(taps2, w_second, frames, rows) + b_second[...]
    result = own[...].astype(jnp.float32).reshape(frames * rows * cols, chans) + second
    out[...] = result.astype(jnp.bfloat16).reshape(frames, rows, cols, chans)


def block(flags, earlier, own, top, bottom, w_first, b_first, w_second, b_second):
    frames, rows, cols, chans = own.shape
    taps = w_first.shape[0] * w_first.shape[1] * w_first.shape[2]
    w_first = w_first.reshape(taps, chans, chans)
    w_second = w_second.reshape(taps, chans, chans)
    positions = (frames + 2) * (rows + 2) * cols + frames * rows * cols
    vmem = pl.BlockSpec(memory_space=pltpu.VMEM)
    return pl.pallas_call(
        block_kernel,
        out_shape=jax.ShapeDtypeStruct(own.shape, own.dtype),
        in_specs=[pl.BlockSpec(memory_space=pltpu.SMEM)] + [vmem] * 8,
        out_specs=vmem,
        scratch_shapes=[
            pltpu.VMEM((2 * frames, rows + 4, cols, chans), jnp.float32),
            pltpu.VMEM((3, 2 * frames, rows + 4, cols, chans), jnp.bfloat16),
            pltpu.VMEM((3, frames + 2, rows + 2, cols, chans), jnp.bfloat16),
        ],
        cost_estimate=pl.CostEstimate(
            flops=2 * positions * taps * chans * chans,
            transcendentals=2 * positions * chans,
            bytes_accessed=2 * (2 * taps * chans * chans + 4 * own.size),
        ),
    )(flags, earlier, own, top, bottom, w_first, b_first.reshape(1, chans), w_second, b_second.reshape(1, chans))


def local(clip_frames, w_first, b_first, w_second, b_second):
    rows = clip_frames.shape[1]
    x = clip_frames
    earlier = neighbour(x, "tm", 1)
    extended = jnp.concatenate([earlier, x], 0)
    top = neighbour(extended[:, rows - 2 :], "height", 1)
    bottom = neighbour(extended[:, :2], "height", -1)
    t, h = lax.axis_index("tm"), lax.axis_index("height")
    flags = jnp.stack([t == 0, h == 0, h == lax.axis_size("height") - 1]).astype(jnp.int32)
    return block(flags, earlier, x, top, bottom, w_first, b_first, w_second, b_second)


def solution(mesh):
    return jax.shard_map(
        local,
        mesh=mesh,
        in_specs=(P(("clips", "tm"), "height", None, None), P(), P(), P(), P()),
        out_specs=P(("clips", "tm"), "height", None, None),
        check_vma=False,
    )
```

```python
import functools

import jax
import jax.numpy as jnp
from jax import lax
from jax.experimental import pallas as pl
from jax.experimental.pallas import tpu as pltpu
from jax.sharding import PartitionSpec as P


def silu(value):
    value = value.astype(jnp.float32)
    return value / (1 + jnp.exp(-value))


def neighbour(value, axis, step):
    size = lax.axis_size(axis)
    pairs = [(i, i + step) for i in range(size) if 0 <= i + step < size]
    return lax.ppermute(value, axis, pairs)


def spread_taps(flat, cols, rows, buf):
    count, lanes = flat.shape
    col = lax.broadcasted_iota(jnp.int32, flat.shape, 0) % cols
    shifted = (
        jnp.where(col == 0, 0.0, pltpu.roll(flat, 1, 0)),
        flat,
        jnp.where(col == cols - 1, 0.0, pltpu.roll(flat, count - 1, 0)),
    )
    frames = buf.shape[0]
    for e in range(3):
        value = shifted[e].astype(jnp.bfloat16).reshape(frames, rows + 2, cols, lanes)
        for b in range(3):
            k = 3 * b + e
            buf[:, :, :, k * lanes : (k + 1) * lanes] = value[:, b : b + rows]


def conv_time_taps(buf, weight, frames):
    rows, cols, depth = buf.shape[1], buf.shape[2], buf.shape[3]
    total = None
    for a in range(3):
        lhs = buf[a : a + frames].reshape(frames * rows * cols, depth)
        term = jnp.dot(lhs, weight[a], preferred_element_type=jnp.float32)
        total = term if total is None else total + term
    return total


def block_kernel(
    flags, earlier, own, top, bottom, w_first, b_first, w_second, b_second, out, field, buf1, gated, buf2
):
    frames, rows, cols, chans = own.shape
    lanes = field.shape[3]
    field[:, :, :, chans:] = jnp.zeros(field.shape[:3] + (lanes - chans,), jnp.float32)
    field[0:frames, 2 : rows + 2, :, 0:chans] = silu(earlier[...])
    field[frames:, 2 : rows + 2, :, 0:chans] = silu(own[...])
    field[:, 0:2, :, 0:chans] = silu(top[...])
    field[:, rows + 2 :, :, 0:chans] = silu(bottom[...])
    spread_taps(field[...].reshape(2 * frames * (rows + 4) * cols, lanes), cols, rows + 2, buf1)
    hidden = conv_time_taps(buf1, w_first, frames + 2) + b_first[...]
    gated[...] = silu(hidden).reshape(frames + 2, rows + 2, cols, lanes)

    @pl.when(flags[0] != 0)
    def _():
        gated[0:2] = jnp.zeros((2, rows + 2, cols, lanes), jnp.float32)

    @pl.when(flags[1] != 0)
    def _():
        gated[:, 0:1] = jnp.zeros((frames + 2, 1, cols, lanes), jnp.float32)

    @pl.when(flags[2] != 0)
    def _():
        gated[:, rows + 1 :] = jnp.zeros((frames + 2, 1, cols, lanes), jnp.float32)

    spread_taps(gated[...].reshape((frames + 2) * (rows + 2) * cols, lanes), cols, rows, buf2)
    second = conv_time_taps(buf2, w_second, frames) + b_second[...]
    result = own[...].astype(jnp.float32).reshape(frames * rows * cols, chans) + second
    out[...] = result.astype(jnp.bfloat16).reshape(frames, rows, cols, chans)


def block(flags, earlier, own, top, bottom, w_first, b_first, w_second, b_second):
    frames, rows, cols, chans = own.shape
    lanes = -(-chans // 256) * 256
    extra = lanes - chans
    w_first = jnp.pad(w_first, ((0, 0),) * 3 + ((0, extra), (0, extra))).reshape(3, 9 * lanes, lanes)
    w_second = jnp.pad(w_second, ((0, 0),) * 3 + ((0, extra), (0, 0))).reshape(3, 9 * lanes, chans)
    b_first = jnp.pad(b_first, (0, extra)).reshape(1, lanes)
    positions = (frames + 2) * (rows + 2) * cols + frames * rows * cols
    vmem = pl.BlockSpec(memory_space=pltpu.VMEM)
    return pl.pallas_call(
        block_kernel,
        out_shape=jax.ShapeDtypeStruct(own.shape, own.dtype),
        in_specs=[pl.BlockSpec(memory_space=pltpu.SMEM)] + [vmem] * 8,
        out_specs=vmem,
        scratch_shapes=[
            pltpu.VMEM((2 * frames, rows + 4, cols, lanes), jnp.float32),
            pltpu.VMEM((2 * frames, rows + 2, cols, 9 * lanes), jnp.bfloat16),
            pltpu.VMEM((frames + 2, rows + 2, cols, lanes), jnp.float32),
            pltpu.VMEM((frames + 2, rows, cols, 9 * lanes), jnp.bfloat16),
        ],
        compiler_params=pltpu.CompilerParams(vmem_limit_bytes=48 * 1024 * 1024),
        cost_estimate=pl.CostEstimate(
            flops=2 * positions * 27 * chans * chans,
            transcendentals=2 * positions * chans,
            bytes_accessed=2 * (54 * lanes * lanes + 4 * own.size),
        ),
    )(flags, earlier, own, top, bottom, w_first, b_first, w_second, b_second.reshape(1, chans))


def local(clip_frames, w_first, b_first, w_second, b_second):
    rows = clip_frames.shape[1]
    x = clip_frames
    earlier = neighbour(x, "tm", 1)
    extended = jnp.concatenate([earlier, x], 0)
    top = neighbour(extended[:, rows - 2 :], "height", 1)
    bottom = neighbour(extended[:, :2], "height", -1)
    t, h = lax.axis_index("tm"), lax.axis_index("height")
    flags = jnp.stack([t == 0, h == 0, h == lax.axis_size("height") - 1]).astype(jnp.int32)
    return block(flags, earlier, x, top, bottom, w_first, b_first, w_second, b_second)


def solution(mesh):
    return jax.shard_map(
        local,
        mesh=mesh,
        in_specs=(P(("clips", "tm"), "height", None, None), P(), P(), P(), P()),
        out_specs=P(("clips", "tm"), "height", None, None),
        check_vma=False,
    )
```

```python
import functools

import jax
import jax.numpy as jnp
from jax import lax
from jax.experimental import pallas as pl
from jax.experimental.pallas import tpu as pltpu
from jax.sharding import PartitionSpec as P


def silu(value):
    value = value.astype(jnp.float32)
    return value / (1 + jnp.exp(-value))


def neighbour(value, axis, step):
    size = lax.axis_size(axis)
    pairs = [(i, i + step) for i in range(size) if 0 <= i + step < size]
    return lax.ppermute(value, axis, pairs)


def spread_taps(flat, cols, rows, buf):
    count, lanes = flat.shape
    col = lax.broadcasted_iota(jnp.int32, flat.shape, 0) % cols
    shifted = (
        jnp.where(col == 0, 0.0, pltpu.roll(flat, 1, 0)),
        flat,
        jnp.where(col == cols - 1, 0.0, pltpu.roll(flat, count - 1, 0)),
    )
    frames = buf.shape[0]
    for e in range(3):
        value = shifted[e].astype(jnp.bfloat16).reshape(frames, rows + 2, cols, lanes)
        for b in range(3):
            k = 3 * b + e
            buf[:, :, :, k * lanes : (k + 1) * lanes] = value[:, b : b + rows]


def conv_time_taps(buf, weight, frames, chains=2):
    rows, cols, depth = buf.shape[1], buf.shape[2], buf.shape[3]
    bounds = [frames * i // chains for i in range(chains + 1)]
    parts = []
    for lo, hi in zip(bounds[:-1], bounds[1:]):
        total = None
        for a in range(3):
            lhs = buf[a + lo : a + hi].reshape((hi - lo) * rows * cols, depth)
            term = jnp.dot(lhs, weight[a], preferred_element_type=jnp.float32)
            total = term if total is None else total + term
        parts.append(total)
    return jnp.concatenate(parts, 0)


def block_kernel(
    flags, earlier, own, top, bottom, w_first, b_first, w_second, b_second, out, field, buf1, gated, buf2
):
    frames, rows, cols, chans = own.shape
    lanes = field.shape[3]
    field[:, :, :, chans:] = jnp.zeros(field.shape[:3] + (lanes - chans,), jnp.float32)
    field[0:frames, 2 : rows + 2, :, 0:chans] = silu(earlier[...])
    field[frames:, 2 : rows + 2, :, 0:chans] = silu(own[...])
    field[:, 0:2, :, 0:chans] = silu(top[...])
    field[:, rows + 2 :, :, 0:chans] = silu(bottom[...])
    spread_taps(field[...].reshape(2 * frames * (rows + 4) * cols, lanes), cols, rows + 2, buf1)
    hidden = conv_time_taps(buf1, w_first, frames + 2) + b_first[...]
    gated[...] = silu(hidden).reshape(frames + 2, rows + 2, cols, lanes)

    @pl.when(flags[0] != 0)
    def _():
        gated[0:2] = jnp.zeros((2, rows + 2, cols, lanes), jnp.float32)

    @pl.when(flags[1] != 0)
    def _():
        gated[:, 0:1] = jnp.zeros((frames + 2, 1, cols, lanes), jnp.float32)

    @pl.when(flags[2] != 0)
    def _():
        gated[:, rows + 1 :] = jnp.zeros((frames + 2, 1, cols, lanes), jnp.float32)

    spread_taps(gated[...].reshape((frames + 2) * (rows + 2) * cols, lanes), cols, rows, buf2)
    second = conv_time_taps(buf2, w_second, frames)[:, 0:chans] + b_second[...]
    result = own[...].astype(jnp.float32).reshape(frames * rows * cols, chans) + second
    out[...] = result.astype(jnp.bfloat16).reshape(frames, rows, cols, chans)


def block(flags, earlier, own, top, bottom, w_first, b_first, w_second, b_second):
    frames, rows, cols, chans = own.shape
    lanes = -(-chans // 256) * 256
    extra = lanes - chans
    w_first = jnp.pad(w_first, ((0, 0),) * 3 + ((0, extra), (0, extra))).reshape(3, 9 * lanes, lanes)
    w_second = jnp.pad(w_second, ((0, 0),) * 3 + ((0, extra), (0, extra))).reshape(3, 9 * lanes, lanes)
    b_first = jnp.pad(b_first, (0, extra)).reshape(1, lanes)
    positions = (frames + 2) * (rows + 2) * cols + frames * rows * cols
    vmem = pl.BlockSpec(memory_space=pltpu.VMEM)
    return pl.pallas_call(
        block_kernel,
        out_shape=jax.ShapeDtypeStruct(own.shape, own.dtype),
        in_specs=[pl.BlockSpec(memory_space=pltpu.SMEM)] + [vmem] * 8,
        out_specs=vmem,
        scratch_shapes=[
            pltpu.VMEM((2 * frames, rows + 4, cols, lanes), jnp.float32),
            pltpu.VMEM((2 * frames, rows + 2, cols, 9 * lanes), jnp.bfloat16),
            pltpu.VMEM((frames + 2, rows + 2, cols, lanes), jnp.float32),
            pltpu.VMEM((frames + 2, rows, cols, 9 * lanes), jnp.bfloat16),
        ],
        compiler_params=pltpu.CompilerParams(vmem_limit_bytes=48 * 1024 * 1024),
        cost_estimate=pl.CostEstimate(
            flops=2 * positions * 27 * chans * chans,
            transcendentals=2 * positions * chans,
            bytes_accessed=2 * (54 * lanes * lanes + 4 * own.size),
        ),
    )(flags, earlier, own, top, bottom, w_first, b_first, w_second, b_second.reshape(1, chans))


def local(clip_frames, w_first, b_first, w_second, b_second):
    rows = clip_frames.shape[1]
    x = clip_frames
    earlier = neighbour(x, "tm", 1)
    extended = jnp.concatenate([earlier, x], 0)
    top = neighbour(extended[:, rows - 2 :], "height", 1)
    bottom = neighbour(extended[:, :2], "height", -1)
    t, h = lax.axis_index("tm"), lax.axis_index("height")
    flags = jnp.stack([t == 0, h == 0, h == lax.axis_size("height") - 1]).astype(jnp.int32)
    return block(flags, earlier, x, top, bottom, w_first, b_first, w_second, b_second)


def solution(mesh):
    return jax.shard_map(
        local,
        mesh=mesh,
        in_specs=(P(("clips", "tm"), "height", None, None), P(), P(), P(), P()),
        out_specs=P(("clips", "tm"), "height", None, None),
        check_vma=False,
    )
```

```python
import functools

import jax
import jax.numpy as jnp
from jax import lax
from jax.experimental import pallas as pl
from jax.experimental.pallas import tpu as pltpu
from jax.sharding import PartitionSpec as P


def silu(value):
    value = value.astype(jnp.float32)
    return value / (1 + jnp.exp(-value))


def neighbour(value, axis, step):
    size = lax.axis_size(axis)
    pairs = [(i, i + step) for i in range(size) if 0 <= i + step < size]
    return lax.ppermute(value, axis, pairs)


def spread_taps(flat, cols, rows, buf):
    count, lanes = flat.shape
    col = lax.broadcasted_iota(jnp.int32, flat.shape, 0) % cols
    shifted = (
        jnp.where(col == 0, 0.0, pltpu.roll(flat, 1, 0)),
        flat,
        jnp.where(col == cols - 1, 0.0, pltpu.roll(flat, count - 1, 0)),
    )
    frames = buf.shape[0]
    for e in range(3):
        value = shifted[e].astype(jnp.bfloat16).reshape(frames, rows + 2, cols, lanes)
        for b in range(3):
            k = 3 * b + e
            buf[:, :, :, k * lanes : (k + 1) * lanes] = value[:, b : b + rows]


def conv_time_taps(buf, weight, frames, chains=2):
    rows, cols, depth = buf.shape[1], buf.shape[2], buf.shape[3]
    bounds = [frames * i // chains for i in range(chains + 1)]
    parts = []
    for lo, hi in zip(bounds[:-1], bounds[1:]):
        total = None
        for a in range(3):
            lhs = buf[a + lo : a + hi].reshape((hi - lo) * rows * cols, depth)
            term = jnp.dot(lhs, weight[a], preferred_element_type=jnp.float32)
            total = term if total is None else total + term
        parts.append(total)
    return jnp.concatenate(parts, 0)


def block_kernel(
    flags, earlier, own, top, bottom, w_first, b_first, w_second, b_second, out, field, buf1, gated, buf2
):
    frames, rows, cols, chans = own.shape
    lanes = field.shape[3]
    field[:, :, :, chans:] = jnp.zeros(field.shape[:3] + (lanes - chans,), jnp.float32)
    field[0:frames, 2 : rows + 2, :, 0:chans] = silu(earlier[...])
    field[frames:, 2 : rows + 2, :, 0:chans] = silu(own[...])
    field[:, 0:2, :, 0:chans] = silu(top[...])
    field[:, rows + 2 :, :, 0:chans] = silu(bottom[...])
    spread_taps(field[...].reshape(2 * frames * (rows + 4) * cols, lanes), cols, rows + 2, buf1)
    hidden = conv_time_taps(buf1, w_first, frames + 2) + b_first[...]
    gated[...] = silu(hidden).reshape(frames + 2, rows + 2, cols, lanes)

    @pl.when(flags[0] != 0)
    def _():
        gated[0:2] = jnp.zeros((2, rows + 2, cols, lanes), jnp.float32)

    @pl.when(flags[1] != 0)
    def _():
        gated[:, 0:1] = jnp.zeros((frames + 2, 1, cols, lanes), jnp.float32)

    @pl.when(flags[2] != 0)
    def _():
        gated[:, rows + 1 :] = jnp.zeros((frames + 2, 1, cols, lanes), jnp.float32)

    spread_taps(gated[...].reshape((frames + 2) * (rows + 2) * cols, lanes), cols, rows, buf2)
    second = conv_time_taps(buf2, w_second, frames)[:, 0:chans] + b_second[...]
    result = own[...].astype(jnp.float32).reshape(frames * rows * cols, chans) + second
    out[...] = result.astype(jnp.bfloat16).reshape(frames, rows, cols, chans)


def block(flags, earlier, own, top, bottom, w_first, b_first, w_second, b_second):
    frames, rows, cols, chans = own.shape
    lanes = -(-chans // 256) * 256
    extra = lanes - chans
    w_first = jnp.pad(w_first, ((0, 0),) * 3 + ((0, extra), (0, extra))).reshape(3, 9 * lanes, lanes)
    w_second = jnp.pad(w_second, ((0, 0),) * 3 + ((0, extra), (0, extra))).reshape(3, 9 * lanes, lanes)
    b_first = jnp.pad(b_first, (0, extra)).reshape(1, lanes)
    positions = (frames + 2) * (rows + 2) * cols + frames * rows * cols
    vmem = pl.BlockSpec(memory_space=pltpu.VMEM)
    return pl.pallas_call(
        block_kernel,
        out_shape=jax.ShapeDtypeStruct(own.shape, own.dtype),
        in_specs=[pl.BlockSpec(memory_space=pltpu.SMEM)] + [vmem] * 8,
        out_specs=vmem,
        scratch_shapes=[
            pltpu.VMEM((2 * frames, rows + 4, cols, lanes), jnp.float32),
            pltpu.VMEM((2 * frames, rows + 2, cols, 9 * lanes), jnp.bfloat16),
            pltpu.VMEM((frames + 2, rows + 2, cols, lanes), jnp.float32),
            pltpu.VMEM((frames + 2, rows, cols, 9 * lanes), jnp.bfloat16),
        ],
        compiler_params=pltpu.CompilerParams(vmem_limit_bytes=48 * 1024 * 1024),
        cost_estimate=pl.CostEstimate(
            flops=2 * positions * 27 * chans * chans,
            transcendentals=2 * positions * chans,
            bytes_accessed=2 * (54 * lanes * lanes + 4 * own.size),
        ),
    )(flags, earlier, own, top, bottom, w_first, b_first, w_second, b_second.reshape(1, chans))


def row_exchange(value, rows_up, rows_down):
    size = lax.axis_size("height")
    h = lax.axis_index("height")
    peer = lax.broadcasted_iota(jnp.int32, (size,) + (1,) * value.ndim, 0)
    send = jnp.where(peer == h + 1, value[:, value.shape[1] - rows_up :][None], 0)
    send = jnp.where(peer == h - 1, value[:, :rows_down][None], send)
    got = lax.all_to_all(send, "height", 0, 0, tiled=False)
    top = lax.dynamic_index_in_dim(got, (h + size - 1) % size, 0, keepdims=False)
    bottom = lax.dynamic_index_in_dim(got, (h + 1) % size, 0, keepdims=False)
    top = jnp.where(h > 0, top, 0)
    bottom = jnp.where(h < size - 1, bottom, 0)
    return top, bottom


def local(clip_frames, w_first, b_first, w_second, b_second):
    x = clip_frames
    earlier = neighbour(x, "tm", 1)
    top, bottom = row_exchange(jnp.concatenate([earlier, x], 0), 2, 2)
    t, h = lax.axis_index("tm"), lax.axis_index("height")
    flags = jnp.stack([t == 0, h == 0, h == lax.axis_size("height") - 1]).astype(jnp.int32)
    return block(flags, earlier, x, top, bottom, w_first, b_first, w_second, b_second)


def solution(mesh):
    return jax.shard_map(
        local,
        mesh=mesh,
        in_specs=(P(("clips", "tm"), "height", None, None), P(), P(), P(), P()),
        out_specs=P(("clips", "tm"), "height", None, None),
        check_vma=False,
    )
```

```python
import functools

import jax
import jax.numpy as jnp
from jax import lax
from jax.experimental import pallas as pl
from jax.experimental.pallas import tpu as pltpu
from jax.sharding import PartitionSpec as P


def silu(value):
    value = value.astype(jnp.float32)
    return value / (1 + jnp.exp(-value))


def neighbour(value, axis, step):
    size = lax.axis_size(axis)
    pairs = [(i, i + step) for i in range(size) if 0 <= i + step < size]
    return lax.ppermute(value, axis, pairs)


def spread_taps(flat, cols, rows, buf):
    count, lanes = flat.shape
    col = lax.broadcasted_iota(jnp.int32, flat.shape, 0) % cols
    shifted = (
        jnp.where(col == 0, 0.0, pltpu.roll(flat, 1, 0)),
        flat,
        jnp.where(col == cols - 1, 0.0, pltpu.roll(flat, count - 1, 0)),
    )
    frames = buf.shape[0]
    view = (frames, rows + 2, cols, 128)
    low = [v[:, 0:128].astype(jnp.bfloat16).reshape(view) for v in shifted]
    high = [v[:, 128:256] for v in shifted]
    turned = [pltpu.roll(v, 64, 1) for v in high]
    for k in range(9):
        b, e = divmod(k, 3)
        buf[:, :, :, 128 * k : 128 * (k + 1)] = low[e][:, b : b + rows]
    for j in range(5):
        b, e = divmod(2 * j, 3)
        packed = high[e].reshape(view)[:, b : b + rows]
        if 2 * j + 1 < 9:
            b, e = divmod(2 * j + 1, 3)
            packed = packed + turned[e].reshape(view)[:, b : b + rows]
        buf[:, :, :, 128 * (9 + j) : 128 * (10 + j)] = packed.astype(jnp.bfloat16)


def dense_weight(weight, lanes):
    taps, chans, out = 9, weight.shape[3], weight.shape[4]
    weight = weight.reshape(3, taps, chans, out)
    low = weight[:, :, 0:128].reshape(3, taps * 128, out)
    high = jnp.pad(weight[:, :, 128:], ((0, 0), (0, 1), (0, 0), (0, 0))).reshape(3, (taps + 1) * (chans - 128), out)
    return jnp.pad(jnp.concatenate([low, high], 1), ((0, 0), (0, 0), (0, lanes - out)))


def conv_time_taps(buf, weight, frames, chains=2):
    rows, cols, depth = buf.shape[1], buf.shape[2], buf.shape[3]
    bounds = [frames * i // chains for i in range(chains + 1)]
    parts = []
    for lo, hi in zip(bounds[:-1], bounds[1:]):
        total = None
        for a in range(3):
            lhs = buf[a + lo : a + hi].reshape((hi - lo) * rows * cols, depth)
            term = jnp.dot(lhs, weight[a], preferred_element_type=jnp.float32)
            total = term if total is None else total + term
        parts.append(total)
    return jnp.concatenate(parts, 0)


def block_kernel(
    flags, earlier, own, top, bottom, w_first, b_first, w_second, b_second, out, field, buf1, gated, buf2
):
    frames, rows, cols, chans = own.shape
    lanes = field.shape[3]
    field[:, :, :, chans:] = jnp.zeros(field.shape[:3] + (lanes - chans,), jnp.float32)
    field[0:frames, 2 : rows + 2, :, 0:chans] = silu(earlier[...])
    field[frames:, 2 : rows + 2, :, 0:chans] = silu(own[...])
    field[:, 0:2, :, 0:chans] = silu(top[...])
    field[:, rows + 2 :, :, 0:chans] = silu(bottom[...])
    spread_taps(field[...].reshape(2 * frames * (rows + 4) * cols, lanes), cols, rows + 2, buf1)
    hidden = conv_time_taps(buf1, w_first, frames + 2) + b_first[...]
    gated[...] = silu(hidden).reshape(frames + 2, rows + 2, cols, lanes)

    @pl.when(flags[0] != 0)
    def _():
        gated[0:2] = jnp.zeros((2, rows + 2, cols, lanes), jnp.float32)

    @pl.when(flags[1] != 0)
    def _():
        gated[:, 0:1] = jnp.zeros((frames + 2, 1, cols, lanes), jnp.float32)

    @pl.when(flags[2] != 0)
    def _():
        gated[:, rows + 1 :] = jnp.zeros((frames + 2, 1, cols, lanes), jnp.float32)

    spread_taps(gated[...].reshape((frames + 2) * (rows + 2) * cols, lanes), cols, rows, buf2)
    second = conv_time_taps(buf2, w_second, frames)[:, 0:chans] + b_second[...]
    result = own[...].astype(jnp.float32).reshape(frames * rows * cols, chans) + second
    out[...] = result.astype(jnp.bfloat16).reshape(frames, rows, cols, chans)


def block(flags, earlier, own, top, bottom, w_first, b_first, w_second, b_second):
    frames, rows, cols, chans = own.shape
    lanes = -(-chans // 256) * 256
    extra = lanes - chans
    w_first = dense_weight(w_first, lanes)
    w_second = dense_weight(w_second, lanes)
    b_first = jnp.pad(b_first, (0, extra)).reshape(1, lanes)
    depth = 9 * 128 + 5 * 128
    positions = (frames + 2) * (rows + 2) * cols + frames * rows * cols
    vmem = pl.BlockSpec(memory_space=pltpu.VMEM)
    return pl.pallas_call(
        block_kernel,
        out_shape=jax.ShapeDtypeStruct(own.shape, own.dtype),
        in_specs=[pl.BlockSpec(memory_space=pltpu.SMEM)] + [vmem] * 8,
        out_specs=vmem,
        scratch_shapes=[
            pltpu.VMEM((2 * frames, rows + 4, cols, lanes), jnp.float32),
            pltpu.VMEM((2 * frames, rows + 2, cols, depth), jnp.bfloat16),
            pltpu.VMEM((frames + 2, rows + 2, cols, lanes), jnp.float32),
            pltpu.VMEM((frames + 2, rows, cols, depth), jnp.bfloat16),
        ],
        compiler_params=pltpu.CompilerParams(vmem_limit_bytes=48 * 1024 * 1024),
        cost_estimate=pl.CostEstimate(
            flops=2 * positions * 27 * chans * chans,
            transcendentals=2 * positions * chans,
            bytes_accessed=2 * (54 * lanes * lanes + 4 * own.size),
        ),
    )(flags, earlier, own, top, bottom, w_first, b_first, w_second, b_second.reshape(1, chans))


def local(clip_frames, w_first, b_first, w_second, b_second):
    rows = clip_frames.shape[1]
    x = clip_frames
    earlier = neighbour(x, "tm", 1)
    extended = jnp.concatenate([earlier, x], 0)
    top = neighbour(extended[:, rows - 2 :], "height", 1)
    bottom = neighbour(extended[:, :2], "height", -1)
    t, h = lax.axis_index("tm"), lax.axis_index("height")
    flags = jnp.stack([t == 0, h == 0, h == lax.axis_size("height") - 1]).astype(jnp.int32)
    return block(flags, earlier, x, top, bottom, w_first, b_first, w_second, b_second)


def solution(mesh):
    return jax.shard_map(
        local,
        mesh=mesh,
        in_specs=(P(("clips", "tm"), "height", None, None), P(), P(), P(), P()),
        out_specs=P(("clips", "tm"), "height", None, None),
        check_vma=False,
    )
```

```python
import functools

import jax
import jax.numpy as jnp
from jax import lax
from jax.experimental import pallas as pl
from jax.experimental.pallas import tpu as pltpu
from jax.sharding import PartitionSpec as P


def silu(value):
    value = value.astype(jnp.float32)
    return value / (1 + jnp.exp(-value))


def neighbour(value, axis, step):
    size = lax.axis_size(axis)
    pairs = [(i, i + step) for i in range(size) if 0 <= i + step < size]
    return lax.ppermute(value, axis, pairs)


def spread_taps(flat, cols, rows, buf):
    count, lanes = flat.shape
    col = lax.broadcasted_iota(jnp.int32, flat.shape, 0) % cols
    shifted = (
        jnp.where(col == 0, 0.0, pltpu.roll(flat, 1, 0)),
        flat,
        jnp.where(col == cols - 1, 0.0, pltpu.roll(flat, count - 1, 0)),
    )
    frames = buf.shape[0]
    view = (frames, rows + 2, cols, 128)
    low = [v[:, 0:128].astype(jnp.bfloat16).reshape(view) for v in shifted]
    high = [v[:, 128:256] for v in shifted]
    turned = [pltpu.roll(v, 64, 1) for v in high]
    for k in range(9):
        b, e = divmod(k, 3)
        buf[:, :, :, 128 * k : 128 * (k + 1)] = low[e][:, b : b + rows]
    for j in range(5):
        b, e = divmod(2 * j, 3)
        packed = high[e].reshape(view)[:, b : b + rows]
        if 2 * j + 1 < 9:
            b, e = divmod(2 * j + 1, 3)
            packed = packed + turned[e].reshape(view)[:, b : b + rows]
        buf[:, :, :, 128 * (9 + j) : 128 * (10 + j)] = packed.astype(jnp.bfloat16)


def dense_rows(weight, a):
    chans = weight.shape[1] // 9
    low = [weight[a, chans * k : chans * k + 128] for k in range(9)]
    high = [weight[a, chans * k + 128 : chans * (k + 1)] for k in range(9)]
    pad = jnp.zeros((128 - (chans - 128), weight.shape[2]), weight.dtype)
    return jnp.concatenate(low + high + [pad], 0)


def conv_time_taps(buf, weight, frames, chains=2):
    rows, cols, depth = buf.shape[1], buf.shape[2], buf.shape[3]
    bounds = [frames * i // chains for i in range(chains + 1)]
    totals = [None] * chains
    for a in range(3):
        rhs = dense_rows(weight, a)
        for i, (lo, hi) in enumerate(zip(bounds[:-1], bounds[1:])):
            lhs = buf[a + lo : a + hi].reshape((hi - lo) * rows * cols, depth)
            term = jnp.dot(lhs, rhs, preferred_element_type=jnp.float32)
            totals[i] = term if totals[i] is None else totals[i] + term
    return jnp.concatenate(totals, 0)


def block_kernel(
    flags, earlier, own, top, bottom, w_first, b_first, w_second, b_second, out, field, buf1, gated, buf2
):
    frames, rows, cols, chans = own.shape
    lanes = field.shape[3]
    field[:, :, :, chans:] = jnp.zeros(field.shape[:3] + (lanes - chans,), jnp.float32)
    field[0:frames, 2 : rows + 2, :, 0:chans] = silu(earlier[...])
    field[frames:, 2 : rows + 2, :, 0:chans] = silu(own[...])
    field[:, 0:2, :, 0:chans] = silu(top[...])
    field[:, rows + 2 :, :, 0:chans] = silu(bottom[...])
    spread_taps(field[...].reshape(2 * frames * (rows + 4) * cols, lanes), cols, rows + 2, buf1)
    hidden = conv_time_taps(buf1, w_first, frames + 2) + b_first[...]
    gated[:, :, :, chans:] = jnp.zeros(gated.shape[:3] + (lanes - chans,), jnp.float32)
    gated[:, :, :, 0:chans] = silu(hidden).reshape(frames + 2, rows + 2, cols, chans)

    @pl.when(flags[0] != 0)
    def _():
        gated[0:2] = jnp.zeros((2, rows + 2, cols, lanes), jnp.float32)

    @pl.when(flags[1] != 0)
    def _():
        gated[:, 0:1] = jnp.zeros((frames + 2, 1, cols, lanes), jnp.float32)

    @pl.when(flags[2] != 0)
    def _():
        gated[:, rows + 1 :] = jnp.zeros((frames + 2, 1, cols, lanes), jnp.float32)

    spread_taps(gated[...].reshape((frames + 2) * (rows + 2) * cols, lanes), cols, rows, buf2)
    second = conv_time_taps(buf2, w_second, frames) + b_second[...]
    result = own[...].astype(jnp.float32).reshape(frames * rows * cols, chans) + second
    out[...] = result.astype(jnp.bfloat16).reshape(frames, rows, cols, chans)


def block(flags, earlier, own, top, bottom, w_first, b_first, w_second, b_second):
    frames, rows, cols, chans = own.shape
    lanes = -(-chans // 256) * 256
    w_first = w_first.reshape(3, 9 * chans, chans)
    w_second = w_second.reshape(3, 9 * chans, chans)
    b_first = b_first.reshape(1, chans)
    depth = 9 * 128 + 5 * 128
    positions = (frames + 2) * (rows + 2) * cols + frames * rows * cols
    vmem = pl.BlockSpec(memory_space=pltpu.VMEM)
    return pl.pallas_call(
        block_kernel,
        out_shape=jax.ShapeDtypeStruct(own.shape, own.dtype),
        in_specs=[pl.BlockSpec(memory_space=pltpu.SMEM)] + [vmem] * 8,
        out_specs=vmem,
        scratch_shapes=[
            pltpu.VMEM((2 * frames, rows + 4, cols, lanes), jnp.float32),
            pltpu.VMEM((2 * frames, rows + 2, cols, depth), jnp.bfloat16),
            pltpu.VMEM((frames + 2, rows + 2, cols, lanes), jnp.float32),
            pltpu.VMEM((frames + 2, rows, cols, depth), jnp.bfloat16),
        ],
        compiler_params=pltpu.CompilerParams(vmem_limit_bytes=48 * 1024 * 1024),
        cost_estimate=pl.CostEstimate(
            flops=2 * positions * 27 * chans * chans,
            transcendentals=2 * positions * chans,
            bytes_accessed=2 * (54 * lanes * lanes + 4 * own.size),
        ),
    )(flags, earlier, own, top, bottom, w_first, b_first, w_second, b_second.reshape(1, chans))


def local(clip_frames, w_first, b_first, w_second, b_second):
    rows = clip_frames.shape[1]
    x = clip_frames
    earlier = neighbour(x, "tm", 1)
    extended = jnp.concatenate([earlier, x], 0)
    top = neighbour(extended[:, rows - 2 :], "height", 1)
    bottom = neighbour(extended[:, :2], "height", -1)
    t, h = lax.axis_index("tm"), lax.axis_index("height")
    flags = jnp.stack([t == 0, h == 0, h == lax.axis_size("height") - 1]).astype(jnp.int32)
    return block(flags, earlier, x, top, bottom, w_first, b_first, w_second, b_second)


def solution(mesh):
    return jax.shard_map(
        local,
        mesh=mesh,
        in_specs=(P(("clips", "tm"), "height", None, None), P(), P(), P(), P()),
        out_specs=P(("clips", "tm"), "height", None, None),
        check_vma=False,
    )
```

```python
import functools

import jax
import jax.numpy as jnp
from jax import lax
from jax.experimental import pallas as pl
from jax.experimental.pallas import tpu as pltpu
from jax.sharding import PartitionSpec as P


def silu(value):
    value = value.astype(jnp.float32)
    return value / (1 + jnp.exp(-value))


def neighbour(value, axis, step):
    size = lax.axis_size(axis)
    pairs = [(i, i + step) for i in range(size) if 0 <= i + step < size]
    return lax.ppermute(value, axis, pairs)


def spread_taps(flat, cols, rows, buf):
    count, lanes = flat.shape
    col = lax.broadcasted_iota(jnp.int32, flat.shape, 0) % cols
    shifted = (
        jnp.where(col == 0, 0.0, pltpu.roll(flat, 1, 0)),
        flat,
        jnp.where(col == cols - 1, 0.0, pltpu.roll(flat, count - 1, 0)),
    )
    frames = buf.shape[0]
    view = (frames, rows + 2, cols, 128)
    low = [v[:, 0:128].astype(jnp.bfloat16).reshape(view) for v in shifted]
    high = [v[:, 128:256] for v in shifted]
    turned = [pltpu.roll(v, 64, 1) for v in high]
    for k in range(9):
        b, e = divmod(k, 3)
        buf[:, :, :, 128 * k : 128 * (k + 1)] = low[e][:, b : b + rows]
    for j in range(5):
        b, e = divmod(2 * j, 3)
        packed = high[e].reshape(view)[:, b : b + rows]
        if 2 * j + 1 < 9:
            b, e = divmod(2 * j + 1, 3)
            packed = packed + turned[e].reshape(view)[:, b : b + rows]
        buf[:, :, :, 128 * (9 + j) : 128 * (10 + j)] = packed.astype(jnp.bfloat16)


def dense_rows(weight, a):
    chans = weight.shape[1] // 9
    low = [weight[a, chans * k : chans * k + 128] for k in range(9)]
    high = [weight[a, chans * k + 128 : chans * (k + 1)] for k in range(9)]
    pad = jnp.zeros((128 - (chans - 128), weight.shape[2]), weight.dtype)
    return jnp.concatenate(low + high + [pad], 0)


def conv_time_taps(buf, weight, frames, chains=2):
    rows, cols, depth = buf.shape[1], buf.shape[2], buf.shape[3]
    bounds = [frames * i // chains for i in range(chains + 1)]
    totals = [None] * chains
    for a in range(3):
        rhs = dense_rows(weight, a)
        for i, (lo, hi) in enumerate(zip(bounds[:-1], bounds[1:])):
            lhs = buf[a + lo : a + hi].reshape((hi - lo) * rows * cols, depth)
            term = jnp.dot(lhs, rhs, preferred_element_type=jnp.float32)
            totals[i] = term if totals[i] is None else totals[i] + term
    return jnp.concatenate(totals, 0)


def block_kernel(
    flags, earlier, top, bottom, own_hbm, w_first_hbm, w_second_hbm, biases_hbm, out,
    own, w_first, w_second, biases, sems, field, buf1, gated, buf2,
):
    copies = [
        pltpu.make_async_copy(src, dst, sems.at[i])
        for i, (src, dst) in enumerate(
            [(own_hbm, own), (biases_hbm, biases), (w_first_hbm, w_first), (w_second_hbm, w_second)]
        )
    ]
    for copy in copies:
        copy.start()
    frames, rows, cols, chans = own.shape
    lanes = field.shape[3]
    field[:, :, :, chans:] = jnp.zeros(field.shape[:3] + (lanes - chans,), jnp.float32)
    field[0:frames, 2 : rows + 2, :, 0:chans] = silu(earlier[...])
    field[:, 0:2, :, 0:chans] = silu(top[...])
    field[:, rows + 2 :, :, 0:chans] = silu(bottom[...])
    copies[0].wait()
    copies[1].wait()
    field[frames:, 2 : rows + 2, :, 0:chans] = silu(own[...])
    spread_taps(field[...].reshape(2 * frames * (rows + 4) * cols, lanes), cols, rows + 2, buf1)
    copies[2].wait()
    hidden = conv_time_taps(buf1, w_first, frames + 2) + biases[0:1, :]
    gated[:, :, :, chans:] = jnp.zeros(gated.shape[:3] + (lanes - chans,), jnp.float32)
    gated[:, :, :, 0:chans] = silu(hidden).reshape(frames + 2, rows + 2, cols, chans)

    @pl.when(flags[0] != 0)
    def _():
        gated[0:2] = jnp.zeros((2, rows + 2, cols, lanes), jnp.float32)

    @pl.when(flags[1] != 0)
    def _():
        gated[:, 0:1] = jnp.zeros((frames + 2, 1, cols, lanes), jnp.float32)

    @pl.when(flags[2] != 0)
    def _():
        gated[:, rows + 1 :] = jnp.zeros((frames + 2, 1, cols, lanes), jnp.float32)

    spread_taps(gated[...].reshape((frames + 2) * (rows + 2) * cols, lanes), cols, rows, buf2)
    copies[3].wait()
    second = conv_time_taps(buf2, w_second, frames) + biases[1:2, :]
    result = own[...].astype(jnp.float32).reshape(frames * rows * cols, chans) + second
    out[...] = result.astype(jnp.bfloat16).reshape(frames, rows, cols, chans)


def block(flags, earlier, own, top, bottom, w_first, b_first, w_second, b_second):
    frames, rows, cols, chans = own.shape
    lanes = -(-chans // 256) * 256
    w_first = w_first.reshape(3, 9 * chans, chans)
    w_second = w_second.reshape(3, 9 * chans, chans)
    biases = jnp.stack([b_first, b_second])
    depth = 9 * 128 + 5 * 128
    positions = (frames + 2) * (rows + 2) * cols + frames * rows * cols
    vmem = pl.BlockSpec(memory_space=pltpu.VMEM)
    hbm = pl.BlockSpec(memory_space=pltpu.HBM)
    return pl.pallas_call(
        block_kernel,
        out_shape=jax.ShapeDtypeStruct(own.shape, own.dtype),
        in_specs=[pl.BlockSpec(memory_space=pltpu.SMEM)] + [vmem] * 3 + [hbm] * 4,
        out_specs=vmem,
        scratch_shapes=[
            pltpu.VMEM(own.shape, own.dtype),
            pltpu.VMEM(w_first.shape, w_first.dtype),
            pltpu.VMEM(w_second.shape, w_second.dtype),
            pltpu.VMEM(biases.shape, biases.dtype),
            pltpu.SemaphoreType.DMA((4,)),
            pltpu.VMEM((2 * frames, rows + 4, cols, lanes), jnp.float32),
            pltpu.VMEM((2 * frames, rows + 2, cols, depth), jnp.bfloat16),
            pltpu.VMEM((frames + 2, rows + 2, cols, lanes), jnp.float32),
            pltpu.VMEM((frames + 2, rows, cols, depth), jnp.bfloat16),
        ],
        cost_estimate=pl.CostEstimate(
            flops=2 * positions * 27 * chans * chans,
            transcendentals=2 * positions * chans,
            bytes_accessed=2 * (54 * chans * chans + 4 * own.size),
        ),
    )(flags, earlier, top, bottom, own, w_first, w_second, biases)


def local(clip_frames, w_first, b_first, w_second, b_second):
    rows = clip_frames.shape[1]
    x = clip_frames
    earlier = neighbour(x, "tm", 1)
    extended = jnp.concatenate([earlier, x], 0)
    top = neighbour(extended[:, rows - 2 :], "height", 1)
    bottom = neighbour(extended[:, :2], "height", -1)
    t, h = lax.axis_index("tm"), lax.axis_index("height")
    flags = jnp.stack([t == 0, h == 0, h == lax.axis_size("height") - 1]).astype(jnp.int32)
    return block(flags, earlier, x, top, bottom, w_first, b_first, w_second, b_second)


def solution(mesh):
    return jax.shard_map(
        local,
        mesh=mesh,
        in_specs=(P(("clips", "tm"), "height", None, None), P(), P(), P(), P()),
        out_specs=P(("clips", "tm"), "height", None, None),
        check_vma=False,
    )
```

```python
import functools

import jax
import jax.numpy as jnp
from jax import lax
from jax.experimental import pallas as pl
from jax.experimental.pallas import tpu as pltpu
from jax.sharding import PartitionSpec as P


def silu(value):
    value = value.astype(jnp.float32)
    return value / (1 + jnp.exp(-value))


def neighbour(value, axis, step):
    size = lax.axis_size(axis)
    pairs = [(i, i + step) for i in range(size) if 0 <= i + step < size]
    return lax.ppermute(value, axis, pairs)


def spread_taps(flat, cols, rows, buf):
    count, lanes = flat.shape
    col = lax.broadcasted_iota(jnp.int32, flat.shape, 0) % cols
    shifted = (
        jnp.where(col == 0, 0.0, pltpu.roll(flat, 1, 0)),
        flat,
        jnp.where(col == cols - 1, 0.0, pltpu.roll(flat, count - 1, 0)),
    )
    frames = buf.shape[0]
    view = (frames, rows + 2, cols, 128)
    low = [v[:, 0:128].astype(jnp.bfloat16).reshape(view) for v in shifted]
    high = [v[:, 128:256] for v in shifted]
    turned = [pltpu.roll(v, 64, 1) for v in high]
    for k in range(9):
        b, e = divmod(k, 3)
        buf[:, :, :, 128 * k : 128 * (k + 1)] = low[e][:, b : b + rows]
    for j in range(5):
        b, e = divmod(2 * j, 3)
        packed = high[e].reshape(view)[:, b : b + rows]
        if 2 * j + 1 < 9:
            b, e = divmod(2 * j + 1, 3)
            packed = packed + turned[e].reshape(view)[:, b : b + rows]
        buf[:, :, :, 128 * (9 + j) : 128 * (10 + j)] = packed.astype(jnp.bfloat16)


def dense_rows(weight, a):
    chans = weight.shape[1] // 9
    low = [weight[a, chans * k : chans * k + 128] for k in range(9)]
    high = [weight[a, chans * k + 128 : chans * (k + 1)] for k in range(9)]
    pad = jnp.zeros((128 - (chans - 128), weight.shape[2]), weight.dtype)
    return jnp.concatenate(low + high + [pad], 0)


def conv_time_taps(buf, weight, frames, chains=2):
    rows, cols, depth = buf.shape[1], buf.shape[2], buf.shape[3]
    bounds = [frames * i // chains for i in range(chains + 1)]
    totals = [None] * chains
    for a in range(3):
        rhs = dense_rows(weight, a)
        for i, (lo, hi) in enumerate(zip(bounds[:-1], bounds[1:])):
            lhs = buf[a + lo : a + hi].reshape((hi - lo) * rows * cols, depth)
            term = jnp.dot(lhs, rhs, preferred_element_type=jnp.float32)
            totals[i] = term if totals[i] is None else totals[i] + term
    return jnp.concatenate(totals, 0)


def block_kernel(
    flags, earlier, own, top, bottom, w_first, b_first, w_second, b_second, out, field, buf1, gated, buf2
):
    frames, rows, cols, chans = own.shape
    lanes = field.shape[3]
    field[:, :, :, chans:] = jnp.zeros(field.shape[:3] + (lanes - chans,), jnp.float32)
    field[0:frames, 2 : rows + 2, :, 0:chans] = silu(earlier[...])
    field[frames:, 2 : rows + 2, :, 0:chans] = silu(own[...])
    field[:, 0:2, :, 0:chans] = silu(top[...])
    field[:, rows + 2 :, :, 0:chans] = silu(bottom[...])
    spread_taps(field[...].reshape(2 * frames * (rows + 4) * cols, lanes), cols, rows + 2, buf1)
    hidden = conv_time_taps(buf1, w_first, frames + 2) + b_first[...]
    gated[...] = silu(hidden).reshape(frames + 2, rows + 2, cols, lanes)

    @pl.when(flags[0] != 0)
    def _():
        gated[0:2] = jnp.zeros((2, rows + 2, cols, lanes), jnp.float32)

    @pl.when(flags[1] != 0)
    def _():
        gated[:, 0:1] = jnp.zeros((frames + 2, 1, cols, lanes), jnp.float32)

    @pl.when(flags[2] != 0)
    def _():
        gated[:, rows + 1 :] = jnp.zeros((frames + 2, 1, cols, lanes), jnp.float32)

    spread_taps(gated[...].reshape((frames + 2) * (rows + 2) * cols, lanes), cols, rows, buf2)
    second = conv_time_taps(buf2, w_second, frames)[:, 0:chans] + b_second[...]
    result = own[...].astype(jnp.float32).reshape(frames * rows * cols, chans) + second
    out[...] = result.astype(jnp.bfloat16).reshape(frames, rows, cols, chans)


def block(flags, earlier, own, top, bottom, w_first, b_first, w_second, b_second):
    frames, rows, cols, chans = own.shape
    lanes = -(-chans // 256) * 256
    w_first = jnp.pad(w_first.reshape(3, 9 * chans, chans), ((0, 0), (0, 0), (0, lanes - chans)))
    w_second = jnp.pad(w_second.reshape(3, 9 * chans, chans), ((0, 0), (0, 0), (0, lanes - chans)))
    b_first = jnp.pad(b_first, (0, lanes - chans)).reshape(1, lanes)
    depth = 9 * 128 + 5 * 128
    positions = (frames + 2) * (rows + 2) * cols + frames * rows * cols
    vmem = pl.BlockSpec(memory_space=pltpu.VMEM)
    return pl.pallas_call(
        block_kernel,
        out_shape=jax.ShapeDtypeStruct(own.shape, own.dtype),
        in_specs=[pl.BlockSpec(memory_space=pltpu.SMEM)] + [vmem] * 8,
        out_specs=vmem,
        scratch_shapes=[
            pltpu.VMEM((2 * frames, rows + 4, cols, lanes), jnp.float32),
            pltpu.VMEM((2 * frames, rows + 2, cols, depth), jnp.bfloat16),
            pltpu.VMEM((frames + 2, rows + 2, cols, lanes), jnp.float32),
            pltpu.VMEM((frames + 2, rows, cols, depth), jnp.bfloat16),
        ],
        compiler_params=pltpu.CompilerParams(vmem_limit_bytes=48 * 1024 * 1024),
        cost_estimate=pl.CostEstimate(
            flops=2 * positions * 27 * chans * chans,
            transcendentals=2 * positions * chans,
            bytes_accessed=2 * (54 * lanes * lanes + 4 * own.size),
        ),
    )(flags, earlier, own, top, bottom, w_first, b_first, w_second, b_second.reshape(1, chans))


def local(clip_frames, w_first, b_first, w_second, b_second):
    rows = clip_frames.shape[1]
    x = clip_frames
    earlier = neighbour(x, "tm", 1)
    extended = jnp.concatenate([earlier, x], 0)
    top = neighbour(extended[:, rows - 2 :], "height", 1)
    bottom = neighbour(extended[:, :2], "height", -1)
    t, h = lax.axis_index("tm"), lax.axis_index("height")
    flags = jnp.stack([t == 0, h == 0, h == lax.axis_size("height") - 1]).astype(jnp.int32)
    return block(flags, earlier, x, top, bottom, w_first, b_first, w_second, b_second)


def solution(mesh):
    return jax.shard_map(
        local,
        mesh=mesh,
        in_specs=(P(("clips", "tm"), "height", None, None), P(), P(), P(), P()),
        out_specs=P(("clips", "tm"), "height", None, None),
        check_vma=False,
    )
```

```python
import functools

import jax
import jax.numpy as jnp
from jax import lax
from jax.experimental import pallas as pl
from jax.experimental.pallas import tpu as pltpu
from jax.sharding import PartitionSpec as P


def silu(value):
    value = value.astype(jnp.float32)
    return value / (1 + jnp.exp(-value))


def neighbour(value, axis, step):
    size = lax.axis_size(axis)
    pairs = [(i, i + step) for i in range(size) if 0 <= i + step < size]
    return lax.ppermute(value, axis, pairs)


def spread_taps(flat, cols, rows, buf):
    count, lanes = flat.shape
    col = lax.broadcasted_iota(jnp.int32, flat.shape, 0) % cols
    shifted = (
        jnp.where(col == 0, 0.0, pltpu.roll(flat, 1, 0)),
        flat,
        jnp.where(col == cols - 1, 0.0, pltpu.roll(flat, count - 1, 0)),
    )
    frames = buf.shape[0]
    view = (frames, rows + 2, cols, 128)
    low = [v[:, 0:128].astype(jnp.bfloat16).reshape(view) for v in shifted]
    high = [v[:, 128:256] for v in shifted]
    turned = [pltpu.roll(v, 64, 1) for v in high]
    for k in range(9):
        b, e = divmod(k, 3)
        buf[:, :, :, 128 * k : 128 * (k + 1)] = low[e][:, b : b + rows]
    for j in range(5):
        b, e = divmod(2 * j, 3)
        packed = high[e].reshape(view)[:, b : b + rows]
        if 2 * j + 1 < 9:
            b, e = divmod(2 * j + 1, 3)
            packed = packed + turned[e].reshape(view)[:, b : b + rows]
        buf[:, :, :, 128 * (9 + j) : 128 * (10 + j)] = packed.astype(jnp.bfloat16)


def dense_rows(weight, a):
    chans = weight.shape[1] // 9
    low = [weight[a, chans * k : chans * k + 128] for k in range(9)]
    high = [weight[a, chans * k + 128 : chans * (k + 1)] for k in range(9)]
    pad = jnp.zeros((128 - (chans - 128), weight.shape[2]), weight.dtype)
    return jnp.concatenate(low + high + [pad], 0)


def conv_time_taps(buf, weight, frames, chains=2):
    rows, cols, depth = buf.shape[1], buf.shape[2], buf.shape[3]
    bounds = [frames * i // chains for i in range(chains + 1)]
    totals = [None] * chains
    for a in range(3):
        rhs = dense_rows(weight, a)
        for i, (lo, hi) in enumerate(zip(bounds[:-1], bounds[1:])):
            lhs = buf[a + lo : a + hi].reshape((hi - lo) * rows * cols, depth)
            term = jnp.dot(lhs, rhs, preferred_element_type=jnp.float32)
            totals[i] = term if totals[i] is None else totals[i] + term
    return jnp.concatenate(totals, 0)


def block_kernel(
    flags, earlier, own, top, bottom, w_first, b_first, w_second, b_second, out, field, buf1, gated, buf2
):
    frames, rows, cols, chans = own.shape
    lanes = field.shape[3]
    field[:, :, :, chans:] = jnp.zeros(field.shape[:3] + (lanes - chans,), jnp.float32)
    field[0:frames, :, :, 0:chans] = silu(earlier[...])
    field[frames:, 2 : rows + 2, :, 0:chans] = silu(own[...])
    field[frames:, 0:2, :, 0:chans] = silu(top[...])
    field[frames:, rows + 2 :, :, 0:chans] = silu(bottom[...])
    spread_taps(field[...].reshape(2 * frames * (rows + 4) * cols, lanes), cols, rows + 2, buf1)
    hidden = conv_time_taps(buf1, w_first, frames + 2) + b_first[...]
    gated[...] = silu(hidden).reshape(frames + 2, rows + 2, cols, lanes)

    @pl.when(flags[0] != 0)
    def _():
        gated[0:2] = jnp.zeros((2, rows + 2, cols, lanes), jnp.float32)

    @pl.when(flags[1] != 0)
    def _():
        gated[:, 0:1] = jnp.zeros((frames + 2, 1, cols, lanes), jnp.float32)

    @pl.when(flags[2] != 0)
    def _():
        gated[:, rows + 1 :] = jnp.zeros((frames + 2, 1, cols, lanes), jnp.float32)

    spread_taps(gated[...].reshape((frames + 2) * (rows + 2) * cols, lanes), cols, rows, buf2)
    second = conv_time_taps(buf2, w_second, frames)[:, 0:chans] + b_second[...]
    result = own[...].astype(jnp.float32).reshape(frames * rows * cols, chans) + second
    out[...] = result.astype(jnp.bfloat16).reshape(frames, rows, cols, chans)


def block(flags, earlier, own, top, bottom, w_first, b_first, w_second, b_second):
    frames, rows, cols, chans = own.shape
    lanes = -(-chans // 256) * 256
    w_first = jnp.pad(w_first.reshape(3, 9 * chans, chans), ((0, 0), (0, 0), (0, lanes - chans)))
    w_second = jnp.pad(w_second.reshape(3, 9 * chans, chans), ((0, 0), (0, 0), (0, lanes - chans)))
    b_first = jnp.pad(b_first, (0, lanes - chans)).reshape(1, lanes)
    depth = 9 * 128 + 5 * 128
    positions = (frames + 2) * (rows + 2) * cols + frames * rows * cols
    vmem = pl.BlockSpec(memory_space=pltpu.VMEM)
    return pl.pallas_call(
        block_kernel,
        out_shape=jax.ShapeDtypeStruct(own.shape, own.dtype),
        in_specs=[pl.BlockSpec(memory_space=pltpu.SMEM)] + [vmem] * 8,
        out_specs=vmem,
        scratch_shapes=[
            pltpu.VMEM((2 * frames, rows + 4, cols, lanes), jnp.float32),
            pltpu.VMEM((2 * frames, rows + 2, cols, depth), jnp.bfloat16),
            pltpu.VMEM((frames + 2, rows + 2, cols, lanes), jnp.float32),
            pltpu.VMEM((frames + 2, rows, cols, depth), jnp.bfloat16),
        ],
        compiler_params=pltpu.CompilerParams(vmem_limit_bytes=48 * 1024 * 1024),
        cost_estimate=pl.CostEstimate(
            flops=2 * positions * 27 * chans * chans,
            transcendentals=2 * positions * chans,
            bytes_accessed=2 * (54 * lanes * lanes + 4 * own.size),
        ),
    )(flags, earlier, own, top, bottom, w_first, b_first, w_second, b_second.reshape(1, chans))


def local(clip_frames, w_first, b_first, w_second, b_second):
    rows = clip_frames.shape[1]
    x = clip_frames
    top = neighbour(x[:, rows - 2 :], "height", 1)
    bottom = neighbour(x[:, :2], "height", -1)
    earlier = neighbour(jnp.concatenate([top, x, bottom], 1), "tm", 1)
    t, h = lax.axis_index("tm"), lax.axis_index("height")
    flags = jnp.stack([t == 0, h == 0, h == lax.axis_size("height") - 1]).astype(jnp.int32)
    return block(flags, earlier, x, top, bottom, w_first, b_first, w_second, b_second)


def solution(mesh):
    return jax.shard_map(
        local,
        mesh=mesh,
        in_specs=(P(("clips", "tm"), "height", None, None), P(), P(), P(), P()),
        out_specs=P(("clips", "tm"), "height", None, None),
        check_vma=False,
    )
```

```python
import functools

import jax
import jax.numpy as jnp
from jax import lax
from jax.experimental import pallas as pl
from jax.experimental.pallas import tpu as pltpu
from jax.sharding import PartitionSpec as P


def silu(value):
    value = value.astype(jnp.float32)
    return value / (1 + jnp.exp(-value))


def silu_tanh(value):
    value = value.astype(jnp.float32)
    half = 0.5 * value
    return half + half * jnp.tanh(half)


def neighbour(value, axis, step):
    size = lax.axis_size(axis)
    pairs = [(i, i + step) for i in range(size) if 0 <= i + step < size]
    return lax.ppermute(value, axis, pairs)


def spread_taps(flat, cols, rows, buf):
    count, lanes = flat.shape
    col = lax.broadcasted_iota(jnp.int32, flat.shape, 0) % cols
    shifted = (
        jnp.where(col == 0, 0.0, pltpu.roll(flat, 1, 0)),
        flat,
        jnp.where(col == cols - 1, 0.0, pltpu.roll(flat, count - 1, 0)),
    )
    frames = buf.shape[0]
    view = (frames, rows + 2, cols, 128)
    low = [v[:, 0:128].astype(jnp.bfloat16).reshape(view) for v in shifted]
    high = [v[:, 128:256] for v in shifted]
    turned = [pltpu.roll(v, 64, 1) for v in high]
    for k in range(9):
        b, e = divmod(k, 3)
        buf[:, :, :, 128 * k : 128 * (k + 1)] = low[e][:, b : b + rows]
    for j in range(5):
        b, e = divmod(2 * j, 3)
        packed = high[e].reshape(view)[:, b : b + rows]
        if 2 * j + 1 < 9:
            b, e = divmod(2 * j + 1, 3)
            packed = packed + turned[e].reshape(view)[:, b : b + rows]
        buf[:, :, :, 128 * (9 + j) : 128 * (10 + j)] = packed.astype(jnp.bfloat16)


def dense_rows(weight, a):
    chans = weight.shape[1] // 9
    low = [weight[a, chans * k : chans * k + 128] for k in range(9)]
    high = [weight[a, chans * k + 128 : chans * (k + 1)] for k in range(9)]
    pad = jnp.zeros((128 - (chans - 128), weight.shape[2]), weight.dtype)
    return jnp.concatenate(low + high + [pad], 0)


def conv_time_taps(buf, weight, frames, chains=2):
    rows, cols, depth = buf.shape[1], buf.shape[2], buf.shape[3]
    bounds = [frames * i // chains for i in range(chains + 1)]
    totals = [None] * chains
    for a in range(3):
        rhs = dense_rows(weight, a)
        for i, (lo, hi) in enumerate(zip(bounds[:-1], bounds[1:])):
            lhs = buf[a + lo : a + hi].reshape((hi - lo) * rows * cols, depth)
            term = jnp.dot(lhs, rhs, preferred_element_type=jnp.float32)
            totals[i] = term if totals[i] is None else totals[i] + term
    return totals, bounds


def block_kernel(
    flags, earlier, own, top, bottom, w_first, b_first, w_second, b_second, out, field, buf1, gated, buf2
):
    frames, rows, cols, chans = own.shape
    lanes = field.shape[3]
    field[:, :, :, chans:] = jnp.zeros(field.shape[:3] + (lanes - chans,), jnp.float32)
    field[0:frames, 2 : rows + 2, :, 0:chans] = silu_tanh(earlier[...])
    field[frames:, 2 : rows + 2, :, 0:chans] = silu_tanh(own[...])
    field[:, 0:2, :, 0:chans] = silu_tanh(top[...])
    field[:, rows + 2 :, :, 0:chans] = silu_tanh(bottom[...])
    spread_taps(field[...].reshape(2 * frames * (rows + 4) * cols, lanes), cols, rows + 2, buf1)
    totals, bounds = conv_time_taps(buf1, w_first, frames + 2)
    for total, lo, hi in zip(totals, bounds[:-1], bounds[1:]):
        gated[lo:hi] = silu_tanh(total + b_first[...]).reshape(hi - lo, rows + 2, cols, lanes)

    @pl.when(flags[0] != 0)
    def _():
        gated[0:2] = jnp.zeros((2, rows + 2, cols, lanes), jnp.float32)

    @pl.when(flags[1] != 0)
    def _():
        gated[:, 0:1] = jnp.zeros((frames + 2, 1, cols, lanes), jnp.float32)

    @pl.when(flags[2] != 0)
    def _():
        gated[:, rows + 1 :] = jnp.zeros((frames + 2, 1, cols, lanes), jnp.float32)

    spread_taps(gated[...].reshape((frames + 2) * (rows + 2) * cols, lanes), cols, rows, buf2)
    second = jnp.concatenate(conv_time_taps(buf2, w_second, frames)[0], 0)[:, 0:chans] + b_second[...]
    result = own[...].astype(jnp.float32).reshape(frames * rows * cols, chans) + second
    out[...] = result.astype(jnp.bfloat16).reshape(frames, rows, cols, chans)


def block(flags, earlier, own, top, bottom, w_first, b_first, w_second, b_second):
    frames, rows, cols, chans = own.shape
    lanes = -(-chans // 256) * 256
    w_first = jnp.pad(w_first.reshape(3, 9 * chans, chans), ((0, 0), (0, 0), (0, lanes - chans)))
    w_second = jnp.pad(w_second.reshape(3, 9 * chans, chans), ((0, 0), (0, 0), (0, lanes - chans)))
    b_first = jnp.pad(b_first, (0, lanes - chans)).reshape(1, lanes)
    depth = 9 * 128 + 5 * 128
    positions = (frames + 2) * (rows + 2) * cols + frames * rows * cols
    vmem = pl.BlockSpec(memory_space=pltpu.VMEM)
    return pl.pallas_call(
        block_kernel,
        out_shape=jax.ShapeDtypeStruct(own.shape, own.dtype),
        in_specs=[pl.BlockSpec(memory_space=pltpu.SMEM)] + [vmem] * 8,
        out_specs=vmem,
        scratch_shapes=[
            pltpu.VMEM((2 * frames, rows + 4, cols, lanes), jnp.float32),
            pltpu.VMEM((2 * frames, rows + 2, cols, depth), jnp.bfloat16),
            pltpu.VMEM((frames + 2, rows + 2, cols, lanes), jnp.float32),
            pltpu.VMEM((frames + 2, rows, cols, depth), jnp.bfloat16),
        ],
        compiler_params=pltpu.CompilerParams(vmem_limit_bytes=48 * 1024 * 1024),
        cost_estimate=pl.CostEstimate(
            flops=2 * positions * 27 * chans * chans,
            transcendentals=2 * positions * chans,
            bytes_accessed=2 * (54 * lanes * lanes + 4 * own.size),
        ),
    )(flags, earlier, own, top, bottom, w_first, b_first, w_second, b_second.reshape(1, chans))


def local(clip_frames, w_first, b_first, w_second, b_second):
    rows = clip_frames.shape[1]
    x = clip_frames
    earlier = neighbour(x, "tm", 1)
    extended = jnp.concatenate([earlier, x], 0)
    top = neighbour(extended[:, rows - 2 :], "height", 1)
    bottom = neighbour(extended[:, :2], "height", -1)
    t, h = lax.axis_index("tm"), lax.axis_index("height")
    flags = jnp.stack([t == 0, h == 0, h == lax.axis_size("height") - 1]).astype(jnp.int32)
    return block(flags, earlier, x, top, bottom, w_first, b_first, w_second, b_second)


def solution(mesh):
    return jax.shard_map(
        local,
        mesh=mesh,
        in_specs=(P(("clips", "tm"), "height", None, None), P(), P(), P(), P()),
        out_specs=P(("clips", "tm"), "height", None, None),
        check_vma=False,
    )
```

```python
import functools

import jax
import jax.numpy as jnp
from jax import lax
from jax.experimental import pallas as pl
from jax.experimental.pallas import tpu as pltpu
from jax.sharding import PartitionSpec as P


def silu(value):
    value = value.astype(jnp.float32)
    return value / (1 + jnp.exp(-value))


def silu_tanh(value):
    value = value.astype(jnp.float32)
    half = 0.5 * value
    return half + half * jnp.tanh(half)


def neighbour(value, axis, step):
    size = lax.axis_size(axis)
    pairs = [(i, i + step) for i in range(size) if 0 <= i + step < size]
    return lax.ppermute(value, axis, pairs)


def spread_taps(flat, cols, rows, buf):
    count, lanes = flat.shape
    col = lax.broadcasted_iota(jnp.int32, flat.shape, 0) % cols
    shifted = (
        jnp.where(col == 0, 0.0, pltpu.roll(flat, 1, 0)),
        flat,
        jnp.where(col == cols - 1, 0.0, pltpu.roll(flat, count - 1, 0)),
    )
    frames = buf.shape[0]
    view = (frames, rows + 2, cols, 128)
    low = [v[:, 0:128].astype(jnp.bfloat16).reshape(view) for v in shifted]
    high = [v[:, 128:256] for v in shifted]
    turned = [pltpu.roll(v, 64, 1) for v in high]
    for k in range(9):
        b, e = divmod(k, 3)
        buf[:, :, :, 128 * k : 128 * (k + 1)] = low[e][:, b : b + rows]
    for j in range(5):
        b, e = divmod(2 * j, 3)
        packed = high[e].reshape(view)[:, b : b + rows]
        if 2 * j + 1 < 9:
            b, e = divmod(2 * j + 1, 3)
            packed = packed + turned[e].reshape(view)[:, b : b + rows]
        buf[:, :, :, 128 * (9 + j) : 128 * (10 + j)] = packed.astype(jnp.bfloat16)


def dense_rows(weight, a):
    chans = weight.shape[1] // 9
    low = [weight[a, chans * k : chans * k + 128] for k in range(9)]
    high = [weight[a, chans * k + 128 : chans * (k + 1)] for k in range(9)]
    pad = jnp.zeros((128 - (chans - 128), weight.shape[2]), weight.dtype)
    return jnp.concatenate(low + high + [pad], 0)


def conv_time_taps(buf, weight, frames, chains=2):
    rows, cols, depth = buf.shape[1], buf.shape[2], buf.shape[3]
    bounds = [frames * i // chains for i in range(chains + 1)]
    totals = [None] * chains
    for a in range(3):
        rhs = dense_rows(weight, a)
        for i, (lo, hi) in enumerate(zip(bounds[:-1], bounds[1:])):
            lhs = buf[a + lo : a + hi].reshape((hi - lo) * rows * cols, depth)
            term = jnp.dot(lhs, rhs, preferred_element_type=jnp.float32)
            totals[i] = term if totals[i] is None else totals[i] + term
    return totals, bounds


def block_kernel(
    flags, earlier, own, top, bottom, earlier_top, earlier_bottom, w_first, b_first, w_second, b_second, out,
    field, buf1, gated, buf2
):
    frames, rows, cols, chans = own.shape
    lanes = field.shape[3]
    field[:, :, :, chans:] = jnp.zeros(field.shape[:3] + (lanes - chans,), jnp.float32)
    field[0:frames, 2 : rows + 2, :, 0:chans] = silu_tanh(earlier[...])
    field[frames:, 2 : rows + 2, :, 0:chans] = silu_tanh(own[...])
    field[0:frames, 0:2, :, 0:chans] = silu_tanh(earlier_top[...])
    field[0:frames, rows + 2 :, :, 0:chans] = silu_tanh(earlier_bottom[...])
    field[frames:, 0:2, :, 0:chans] = silu_tanh(top[...])
    field[frames:, rows + 2 :, :, 0:chans] = silu_tanh(bottom[...])
    spread_taps(field[...].reshape(2 * frames * (rows + 4) * cols, lanes), cols, rows + 2, buf1)
    totals, bounds = conv_time_taps(buf1, w_first, frames + 2)
    for total, lo, hi in zip(totals, bounds[:-1], bounds[1:]):
        gated[lo:hi] = silu_tanh(total + b_first[...]).reshape(hi - lo, rows + 2, cols, lanes)

    @pl.when(flags[0] != 0)
    def _():
        gated[0:2] = jnp.zeros((2, rows + 2, cols, lanes), jnp.float32)

    @pl.when(flags[1] != 0)
    def _():
        gated[:, 0:1] = jnp.zeros((frames + 2, 1, cols, lanes), jnp.float32)

    @pl.when(flags[2] != 0)
    def _():
        gated[:, rows + 1 :] = jnp.zeros((frames + 2, 1, cols, lanes), jnp.float32)

    spread_taps(gated[...].reshape((frames + 2) * (rows + 2) * cols, lanes), cols, rows, buf2)
    second = jnp.concatenate(conv_time_taps(buf2, w_second, frames)[0], 0)[:, 0:chans] + b_second[...]
    result = own[...].astype(jnp.float32).reshape(frames * rows * cols, chans) + second
    out[...] = result.astype(jnp.bfloat16).reshape(frames, rows, cols, chans)


def block(flags, earlier, own, top, bottom, earlier_top, earlier_bottom, w_first, b_first, w_second, b_second):
    frames, rows, cols, chans = own.shape
    lanes = -(-chans // 256) * 256
    w_first = jnp.pad(w_first.reshape(3, 9 * chans, chans), ((0, 0), (0, 0), (0, lanes - chans)))
    w_second = jnp.pad(w_second.reshape(3, 9 * chans, chans), ((0, 0), (0, 0), (0, lanes - chans)))
    b_first = jnp.pad(b_first, (0, lanes - chans)).reshape(1, lanes)
    depth = 9 * 128 + 5 * 128
    positions = (frames + 2) * (rows + 2) * cols + frames * rows * cols
    vmem = pl.BlockSpec(memory_space=pltpu.VMEM)
    return pl.pallas_call(
        block_kernel,
        out_shape=jax.ShapeDtypeStruct(own.shape, own.dtype),
        in_specs=[pl.BlockSpec(memory_space=pltpu.SMEM)] + [vmem] * 10,
        out_specs=vmem,
        scratch_shapes=[
            pltpu.VMEM((2 * frames, rows + 4, cols, lanes), jnp.float32),
            pltpu.VMEM((2 * frames, rows + 2, cols, depth), jnp.bfloat16),
            pltpu.VMEM((frames + 2, rows + 2, cols, lanes), jnp.float32),
            pltpu.VMEM((frames + 2, rows, cols, depth), jnp.bfloat16),
        ],
        compiler_params=pltpu.CompilerParams(vmem_limit_bytes=48 * 1024 * 1024),
        cost_estimate=pl.CostEstimate(
            flops=2 * positions * 27 * chans * chans,
            transcendentals=2 * positions * chans,
            bytes_accessed=2 * (54 * lanes * lanes + 4 * own.size),
        ),
    )(flags, earlier, own, top, bottom, earlier_top, earlier_bottom, w_first, b_first, w_second, b_second.reshape(1, chans))


def diagonal(value, step):
    frames, heights = lax.axis_size("tm"), lax.axis_size("height")
    pairs = [
        (t * heights + h, (t + 1) * heights + h + step)
        for t in range(frames - 1)
        for h in range(heights)
        if 0 <= h + step < heights
    ]
    return lax.ppermute(value, ("tm", "height"), pairs)


def local(clip_frames, w_first, b_first, w_second, b_second):
    rows = clip_frames.shape[1]
    x = clip_frames
    earlier = neighbour(x, "tm", 1)
    top = neighbour(x[:, rows - 2 :], "height", 1)
    bottom = neighbour(x[:, :2], "height", -1)
    earlier_top = diagonal(x[:, rows - 2 :], 1)
    earlier_bottom = diagonal(x[:, :2], -1)
    t, h = lax.axis_index("tm"), lax.axis_index("height")
    flags = jnp.stack([t == 0, h == 0, h == lax.axis_size("height") - 1]).astype(jnp.int32)
    return block(flags, earlier, x, top, bottom, earlier_top, earlier_bottom, w_first, b_first, w_second, b_second)


def solution(mesh):
    return jax.shard_map(
        local,
        mesh=mesh,
        in_specs=(P(("clips", "tm"), "height", None, None), P(), P(), P(), P()),
        out_specs=P(("clips", "tm"), "height", None, None),
        check_vma=False,
    )
```

```python
import functools

import jax
import jax.numpy as jnp
from jax import lax
from jax.experimental import pallas as pl
from jax.experimental.pallas import tpu as pltpu
from jax.sharding import PartitionSpec as P


def silu(value):
    value = value.astype(jnp.float32)
    return value / (1 + jnp.exp(-value))


def silu_tanh(value):
    value = value.astype(jnp.float32)
    half = 0.5 * value
    return half + half * jnp.tanh(half)


def neighbour(value, axis, step):
    size = lax.axis_size(axis)
    pairs = [(i, i + step) for i in range(size) if 0 <= i + step < size]
    return lax.ppermute(value, axis, pairs)


def spread_taps(flat, cols, rows, buf):
    count, lanes = flat.shape
    col = lax.broadcasted_iota(jnp.int32, flat.shape, 0) % cols
    shifted = (
        jnp.where(col == 0, 0.0, pltpu.roll(flat, 1, 0)),
        flat,
        jnp.where(col == cols - 1, 0.0, pltpu.roll(flat, count - 1, 0)),
    )
    frames = buf.shape[0]
    view = (frames, rows + 2, cols, 128)
    low = [v[:, 0:128].astype(jnp.bfloat16).reshape(view) for v in shifted]
    high = [v[:, 128:256] for v in shifted]
    turned = [pltpu.roll(v, 64, 1) for v in high]
    for k in range(9):
        b, e = divmod(k, 3)
        buf[:, :, :, 128 * k : 128 * (k + 1)] = low[e][:, b : b + rows]
    for j in range(5):
        b, e = divmod(2 * j, 3)
        packed = high[e].reshape(view)[:, b : b + rows]
        if 2 * j + 1 < 9:
            b, e = divmod(2 * j + 1, 3)
            packed = packed + turned[e].reshape(view)[:, b : b + rows]
        buf[:, :, :, 128 * (9 + j) : 128 * (10 + j)] = packed.astype(jnp.bfloat16)


def dense_rows(weight, a):
    chans = weight.shape[1] // 9
    low = [weight[a, chans * k : chans * k + 128] for k in range(9)]
    high = [weight[a, chans * k + 128 : chans * (k + 1)] for k in range(9)]
    pad = jnp.zeros((128 - (chans - 128), weight.shape[2]), weight.dtype)
    return jnp.concatenate(low + high + [pad], 0)


def conv_time_taps(buf, weight, frames, chains=2):
    rows, cols, depth = buf.shape[1], buf.shape[2], buf.shape[3]
    bounds = [frames * i // chains for i in range(chains + 1)]
    totals = [None] * chains
    for a in range(3):
        rhs = dense_rows(weight, a)
        for i, (lo, hi) in enumerate(zip(bounds[:-1], bounds[1:])):
            lhs = buf[a + lo : a + hi].reshape((hi - lo) * rows * cols, depth)
            term = jnp.dot(lhs, rhs, preferred_element_type=jnp.float32)
            totals[i] = term if totals[i] is None else totals[i] + term
    return totals, bounds


def block_kernel(
    flags, earlier, own, top, bottom, earlier_edges, w_first, b_first, w_second, b_second, out,
    field, buf1, gated, buf2
):
    frames, rows, cols, chans = own.shape
    lanes = field.shape[3]
    field[:, :, :, chans:] = jnp.zeros(field.shape[:3] + (lanes - chans,), jnp.float32)
    field[0:frames, 2 : rows + 2, :, 0:chans] = silu_tanh(earlier[...])
    field[frames:, 2 : rows + 2, :, 0:chans] = silu_tanh(own[...])
    field[0:frames, 0:2, :, 0:chans] = silu_tanh(earlier_edges[:, 0:2])
    field[0:frames, rows + 2 :, :, 0:chans] = silu_tanh(earlier_edges[:, 2:4])
    field[frames:, 0:2, :, 0:chans] = silu_tanh(top[...])
    field[frames:, rows + 2 :, :, 0:chans] = silu_tanh(bottom[...])
    spread_taps(field[...].reshape(2 * frames * (rows + 4) * cols, lanes), cols, rows + 2, buf1)
    totals, bounds = conv_time_taps(buf1, w_first, frames + 2)
    for total, lo, hi in zip(totals, bounds[:-1], bounds[1:]):
        gated[lo:hi] = silu_tanh(total + b_first[...]).reshape(hi - lo, rows + 2, cols, lanes)

    @pl.when(flags[0] != 0)
    def _():
        gated[0:2] = jnp.zeros((2, rows + 2, cols, lanes), jnp.float32)

    @pl.when(flags[1] != 0)
    def _():
        gated[:, 0:1] = jnp.zeros((frames + 2, 1, cols, lanes), jnp.float32)

    @pl.when(flags[2] != 0)
    def _():
        gated[:, rows + 1 :] = jnp.zeros((frames + 2, 1, cols, lanes), jnp.float32)

    spread_taps(gated[...].reshape((frames + 2) * (rows + 2) * cols, lanes), cols, rows, buf2)
    second = jnp.concatenate(conv_time_taps(buf2, w_second, frames)[0], 0)[:, 0:chans] + b_second[...]
    result = own[...].astype(jnp.float32).reshape(frames * rows * cols, chans) + second
    out[...] = result.astype(jnp.bfloat16).reshape(frames, rows, cols, chans)


def block(flags, earlier, own, top, bottom, earlier_edges, w_first, b_first, w_second, b_second):
    frames, rows, cols, chans = own.shape
    lanes = -(-chans // 256) * 256
    w_first = jnp.pad(w_first.reshape(3, 9 * chans, chans), ((0, 0), (0, 0), (0, lanes - chans)))
    w_second = jnp.pad(w_second.reshape(3, 9 * chans, chans), ((0, 0), (0, 0), (0, lanes - chans)))
    b_first = jnp.pad(b_first, (0, lanes - chans)).reshape(1, lanes)
    depth = 9 * 128 + 5 * 128
    positions = (frames + 2) * (rows + 2) * cols + frames * rows * cols
    vmem = pl.BlockSpec(memory_space=pltpu.VMEM)
    return pl.pallas_call(
        block_kernel,
        out_shape=jax.ShapeDtypeStruct(own.shape, own.dtype),
        in_specs=[pl.BlockSpec(memory_space=pltpu.SMEM)] + [vmem] * 9,
        out_specs=vmem,
        scratch_shapes=[
            pltpu.VMEM((2 * frames, rows + 4, cols, lanes), jnp.float32),
            pltpu.VMEM((2 * frames, rows + 2, cols, depth), jnp.bfloat16),
            pltpu.VMEM((frames + 2, rows + 2, cols, lanes), jnp.float32),
            pltpu.VMEM((frames + 2, rows, cols, depth), jnp.bfloat16),
        ],
        compiler_params=pltpu.CompilerParams(vmem_limit_bytes=48 * 1024 * 1024),
        cost_estimate=pl.CostEstimate(
            flops=2 * positions * 27 * chans * chans,
            transcendentals=2 * positions * chans,
            bytes_accessed=2 * (54 * lanes * lanes + 4 * own.size),
        ),
    )(flags, earlier, own, top, bottom, earlier_edges, w_first, b_first, w_second, b_second.reshape(1, chans))


def local(clip_frames, w_first, b_first, w_second, b_second):
    rows = clip_frames.shape[1]
    x = clip_frames
    earlier = neighbour(x, "tm", 1)
    top = neighbour(x[:, rows - 2 :], "height", 1)
    bottom = neighbour(x[:, :2], "height", -1)
    earlier_edges = neighbour(jnp.concatenate([top, bottom], 1), "tm", 1)
    t, h = lax.axis_index("tm"), lax.axis_index("height")
    flags = jnp.stack([t == 0, h == 0, h == lax.axis_size("height") - 1]).astype(jnp.int32)
    return block(flags, earlier, x, top, bottom, earlier_edges, w_first, b_first, w_second, b_second)


def solution(mesh):
    return jax.shard_map(
        local,
        mesh=mesh,
        in_specs=(P(("clips", "tm"), "height", None, None), P(), P(), P(), P()),
        out_specs=P(("clips", "tm"), "height", None, None),
        check_vma=False,
    )
```
